128 devices in a mesh: dp: 4 (over z_hi, core), point: 32 (over x, z_lo, y).
Axes of the slice: x: 4, y: 4, z: 4 (z_hi: 2, z_lo: 2; z = z_hi * 2 + z_lo), core: 2. Of those that a mesh axis runs over, the one named last changes fastest.
Arguments:
- points: bfloat16 [1048576, 256], P(('dp', 'point')), parts along dimension 0, may hold values from -6 to 6
- tree_order: int32 [1048576], P(('dp', 'point')), parts along dimension 0, may hold values from 0 to 262143, as said below
- ball_counts: int32 [4096], P(('dp', 'point')), parts along dimension 0, may hold values from 64 to 256, as said below
- ball_proj: bfloat16 [3, 256, 256], replicated
- ball_out: bfloat16 [256, 256], replicated, may hold values from -0.375 to 0.375
- pool_weight: bfloat16 [16384, 256], replicated, may hold values from -0.046875 to 0.046875
- coarse_proj: bfloat16 [3, 256, 256], replicated
- coarse_out: bfloat16 [256, 256], replicated, may hold values from -6 to 6
- global_proj: bfloat16 [3, 256, 256], replicated
- global_out: bfloat16 [256, 256], replicated, may hold values from -6 to 6
- unpool_weight: bfloat16 [256, 16384], replicated, may hold values from -0.125 to 0.125
- mlp_in: bfloat16 [256, 1024], replicated, may hold values from -0.375 to 0.375
- mlp_out: bfloat16 [1024, 256], replicated, may hold values from -0.1875 to 0.1875
Outputs:
- result: bfloat16 [1048576, 256], P(('dp', 'point')), parts along dimension 0
The draws below stay inside these ranges and needn't reach their ends.
There are 4 independent parts, one for each index of `dp`. The reference program is written for one: setup_inputs(seed, part) draws one part's arguments, and reference() takes and returns one part's arrays. A program takes and returns all parts, laid end to end along the dimension named above; an argument that names none is the same for every part. Nothing has to cross between parts.
Inputs may be any that keep to these rules, and one draw needn't show every extreme that they name: `tree_order`: each block of 8192 slots takes a permutation of the same block of rows. `ball_counts`: live points come first in each ball; every block of 8192 slots holds a full ball.
All inputs are finite; a program needn't handle non-finite values.
Results may differ from the reference program's by a relative error of at most 0.03.
Values may be sent and summed in bfloat16 or wider, within the bound.
No kernel may reach another device: no remote copies, remote signals or barrier semaphores. Data moves between devices by JAX's collectives and lax.ppermute only.
A program may use at most 256 MiB of HBM per device.

```python
import math
import jax
import jax.numpy as jnp
import numpy as np
from jax import lax

D = 256
HEADS = 8
FF = 1024
BALL = 256
POOL = 64
TOK_DEV = 8192
TOKENS = 262144
COARSE_DEV = 128
COARSE = 4096
LEVELS = 5
N_POINT = 32


def draw_tree_order(key, part):
    blocks = TOKENS // TOK_DEV
    key_list = jax.random.split(jax.random.fold_in(key, 11), blocks)
    local_order = jax.vmap(lambda subkey: jax.random.permutation(subkey, TOK_DEV))(key_list)
    offsets = (jnp.arange(blocks) * TOK_DEV)[:, None]
    return (local_order + offsets).reshape(-1).astype(jnp.int32)


def draw_ball_counts(key, part):
    blocks = TOKENS // TOK_DEV
    per_block = TOK_DEV // BALL
    first, second = jax.random.split(jax.random.fold_in(key, 12))
    drawn = jax.random.randint(first, (blocks, per_block), BALL // 4, BALL + 1)
    chosen = jax.random.randint(second, (blocks, 1), 0, per_block)
    full_ball = jnp.arange(per_block)[None, :] == chosen
    return jnp.where(full_ball, BALL, drawn).reshape(-1).astype(jnp.int32)


def projection_draw(key, salt):
    first, second, third = jax.random.split(jax.random.fold_in(key, salt), 3)
    factor = 1.0 / math.sqrt(D)
    shared = jax.random.normal(first, (D, D), jnp.float32) * factor
    other = jax.random.normal(second, (D, D), jnp.float32) * factor
    values = jax.random.normal(third, (D, D), jnp.float32) * factor
    q_part = shared
    k_part = other
    return jnp.stack([q_part, k_part, values]).astype(jnp.bfloat16)


def draw_ball_proj(key, part):
    return projection_draw(key, 21)


def draw_coarse_proj(key, part):
    return projection_draw(key, 22)


def draw_global_proj(key, part):
    return projection_draw(key, 23)


def shard_levels(rng, shape, cuts, low, largest):
    gain, own = 1.0, jax.random.fold_in(rng, 6)
    for axis_at, parts in cuts:
        draws = jnp.exp(jax.random.uniform(jax.random.fold_in(own, axis_at), (parts,), jnp.float32, low / len(cuts), largest / len(cuts)))
        gain = gain * jnp.repeat(draws, shape[axis_at] // parts).reshape([-1 if axis == axis_at else 1 for axis in range(len(shape))])
    return gain


def scatter_about(stream_key, extent, deviation, bound, cuts=(), kind=jnp.bfloat16):
    gain = shard_levels(stream_key, extent, cuts, -0.22, 0.18) if cuts else 1.0
    result = jax.random.normal(stream_key, extent, jnp.float32) * deviation * gain
    return jnp.minimum(jnp.maximum(result, -bound), bound).astype(kind)


def setup_inputs(seed: int = 0, part: int = 0) -> dict:
    keys = jax.random.split(jax.random.key(seed), 14)
    part_keys = jax.random.split(jax.random.fold_in(keys[13], part), 14)
    points = scatter_about(part_keys[0], (TOKENS, D), 1.0, 6.0, ((0, 32),))
    tree_order = draw_tree_order(jax.random.fold_in(jax.random.fold_in(keys[13], part), 71), part)
    ball_counts = draw_ball_counts(jax.random.fold_in(jax.random.fold_in(keys[13], part), 71), part)
    ball_proj = draw_ball_proj(jax.random.fold_in(keys[13], 71), part)
    ball_out = scatter_about(keys[4], (D, D), D ** -0.5, 0.375)
    pool_weight = scatter_about(keys[5], (POOL * D, D), (POOL * D) ** -0.5, 0.046875)
    coarse_proj = draw_coarse_proj(jax.random.fold_in(keys[13], 71), part)
    coarse_out = scatter_about(keys[7], (D, D), ((2 * COARSE_DEV / D) ** 0.5), 6.0)
    global_proj = draw_global_proj(jax.random.fold_in(keys[13], 71), part)
    global_out = scatter_about(keys[9], (D, D), (0.5 * (COARSE / D) ** 0.5), 6.0)
    unpool_weight = scatter_about(keys[10], (D, POOL * D), ((8 / COARSE_DEV) ** 0.75 / D ** 0.5), 0.125)
    mlp_in = scatter_about(keys[11], (D, FF), D ** -0.5, 0.375)
    mlp_out = scatter_about(keys[12], (FF, D), FF ** -0.5, 0.1875)
    return dict(points=points, tree_order=tree_order, ball_counts=ball_counts, ball_proj=ball_proj, ball_out=ball_out, pool_weight=pool_weight, coarse_proj=coarse_proj, coarse_out=coarse_out, global_proj=global_proj, global_out=global_out, unpool_weight=unpool_weight, mlp_in=mlp_in, mlp_out=mlp_out)


EPSILON = 1e-05

def normalize(inputs):
    inputs = inputs.astype(jnp.float32)
    center = inputs - lax.optimization_barrier(jnp.mean(inputs, axis=-1, keepdims=True))
    spread = lax.optimization_barrier(jnp.mean(center * center, axis=-1, keepdims=True))
    return (center * lax.rsqrt(spread + EPSILON)).astype(jnp.bfloat16)

def project(inputs, weight):
    return jnp.dot(inputs, weight, preferred_element_type=jnp.float32).astype(jnp.bfloat16)

def attend(queries, key_rows, value_rows, valid, head_count):
    groups, q_rows, feature = queries.shape
    k_rows = key_rows.shape[1]
    head_size = feature // head_count
    q_heads = queries.astype(jnp.float32).reshape(groups, q_rows, head_count, head_size)
    k_heads = key_rows.astype(jnp.float32).reshape(groups, k_rows, head_count, head_size)
    v_heads = value_rows.astype(jnp.float32).reshape(groups, k_rows, head_count, head_size)
    scores = jnp.einsum('bqhd,bkhd->bhqk', q_heads, k_heads) / math.sqrt(head_size)
    if valid is not None:
        scores = jnp.where(valid[:, None, None, :], scores, -1e+30)
    row_max = lax.optimization_barrier(jnp.max(scores, axis=-1, keepdims=True))
    expo = jnp.exp(scores - row_max)
    attn_probs = (expo / lax.optimization_barrier(jnp.sum(expo, axis=-1, keepdims=True))).astype(jnp.bfloat16)
    mixed = jnp.einsum('bhqk,bkhd->bqhd', attn_probs.astype(jnp.float32), v_heads)
    return mixed.reshape(groups, q_rows, feature).astype(jnp.bfloat16)

def ball_section(tree_rows, live_mask, ball_proj, ball_out):
    row_count, feature = tree_rows.shape
    normed = normalize(tree_rows)
    queries = project(normed, ball_proj[0])
    key_rows = project(normed, ball_proj[1])
    value_rows = project(normed, ball_proj[2])
    groups = row_count // BALL
    mixed = attend(queries.reshape(groups, BALL, feature), key_rows.reshape(groups, BALL, feature), value_rows.reshape(groups, BALL, feature), live_mask.reshape(groups, BALL), HEADS)
    fine = tree_rows.astype(jnp.float32) + jnp.dot(mixed.reshape(row_count, feature), ball_out, preferred_element_type=jnp.float32)
    return fine.astype(jnp.bfloat16)

def fine_section(tree_rows, live_mask, ball_proj, ball_out, pool_weight, mlp_in, mlp_out):
    row_count, feature = tree_rows.shape
    fine = ball_section(tree_rows, live_mask, ball_proj, ball_out)
    masked = jnp.where(live_mask[:, None], fine, jnp.zeros((), jnp.bfloat16))
    pooled = jnp.dot(masked.reshape(row_count // POOL, POOL * feature), pool_weight, preferred_element_type=jnp.float32)
    expanded = jax.nn.gelu(jnp.dot(normalize(fine), mlp_in, preferred_element_type=jnp.float32), approximate=True).astype(jnp.bfloat16)
    refined = fine.astype(jnp.float32) + jnp.dot(expanded, mlp_out, preferred_element_type=jnp.float32)
    return (pooled, refined)

def coarse_qkv(coarse_state, weights):
    normed = normalize(coarse_state)
    return (project(normed, weights[0]), project(normed, weights[1]), project(normed, weights[2]))

def coarse_update(coarse_state, queries, key_rows, value_rows, out_weight):
    mixed = attend(queries, key_rows, value_rows, None, HEADS)
    return coarse_state + jnp.dot(mixed, out_weight, preferred_element_type=jnp.float32)

def run_levels(coarse_state, coarse_proj, coarse_out, level_count):
    block_ids = np.arange(coarse_state.shape[0])
    for level_index in range(level_count):
        queries, key_rows, value_rows = coarse_qkv(coarse_state, coarse_proj)
        partner = block_ids ^ 1 << level_index
        coarse_state = coarse_update(coarse_state, queries, jnp.concatenate([key_rows, key_rows[partner]], axis=1), jnp.concatenate([value_rows, value_rows[partner]], axis=1), coarse_out)
    return coarse_state

def reference(points, tree_order, ball_counts, ball_proj, ball_out, pool_weight, coarse_proj, coarse_out, global_proj, global_out, unpool_weight, mlp_in, mlp_out):
    tree_rows = jnp.take(points, tree_order.astype(jnp.int32), axis=0)
    live_mask = (jnp.arange(BALL, dtype=jnp.int32)[None, :] < ball_counts[:, None]).reshape(-1)

    def one_block(pieces):
        return fine_section(pieces[0], pieces[1], ball_proj, ball_out, pool_weight, mlp_in, mlp_out)
    pooled, refined = lax.map(one_block, (tree_rows.reshape(N_POINT, TOK_DEV, D), live_mask.reshape(N_POINT, TOK_DEV)))
    coarse_state = run_levels(pooled, coarse_proj, coarse_out, LEVELS)
    queries, key_rows, value_rows = coarse_qkv(coarse_state, global_proj)
    mixed = attend(queries.reshape(1, COARSE, D), key_rows.reshape(1, COARSE, D), value_rows.reshape(1, COARSE, D), None, HEADS)
    summary = (coarse_state.reshape(1, COARSE, D) + jnp.dot(mixed, global_out, preferred_element_type=jnp.float32)).astype(jnp.bfloat16)
    unpooled = jnp.dot(summary.reshape(COARSE, D), unpool_weight, preferred_element_type=jnp.float32).reshape(TOKENS, D)
    total = refined.reshape(TOKENS, D) + unpooled
    return jnp.where(live_mask[:, None], total, 0.0).astype(jnp.bfloat16)
```

```python
import math

import jax
import jax.numpy as jnp
from jax import lax
from jax.experimental import pallas as pl
from jax.experimental.pallas import tpu as pltpu
from jax.sharding import PartitionSpec as P

HEADS = 8
BALL = 256
POOL = 64


EPSILON = 1e-05
GATHER_ORDER = (1, 4, 0, 2, 3)


def _norm(x):
    center = x - jnp.mean(x, axis=-1, keepdims=True)
    spread = jnp.mean(center * center, axis=-1, keepdims=True)
    return (center * lax.rsqrt(spread + EPSILON)).astype(jnp.bfloat16)


def _ball_kernel(counts_ref, x_ref, proj_ref, wo_ref, w1_ref, w2_ref, masked_ref, refined_ref):
    count = counts_ref[pl.program_id(0)]
    x = x_ref[...].astype(jnp.float32)
    feature = x.shape[-1]
    head_size = feature // HEADS
    normed = _norm(x)
    q = jnp.dot(normed, proj_ref[0], preferred_element_type=jnp.float32).astype(jnp.bfloat16)
    k = jnp.dot(normed, proj_ref[1], preferred_element_type=jnp.float32).astype(jnp.bfloat16)
    v = jnp.dot(normed, proj_ref[2], preferred_element_type=jnp.float32).astype(jnp.bfloat16)
    key_live = lax.broadcasted_iota(jnp.int32, (1, BALL), 1) < count
    lane = lax.broadcasted_iota(jnp.int32, (1, feature), 1)
    scale = 1.0 / math.sqrt(head_size)
    mixed = jnp.zeros((BALL, feature), jnp.float32)
    for h in range(HEADS):
        in_head = (lane >= h * head_size) & (lane < (h + 1) * head_size)
        qh = jnp.where(in_head, q, jnp.zeros((), jnp.bfloat16))
        vh = jnp.where(in_head, v, jnp.zeros((), jnp.bfloat16))
        scores = lax.dot_general(qh, k, (((1,), (1,)), ((), ())), preferred_element_type=jnp.float32) * scale
        scores = jnp.where(key_live, scores, -1e30)
        row_max = jnp.max(scores, axis=-1, keepdims=True)
        expo = jnp.exp(scores - row_max)
        probs = (expo * (1.0 / jnp.sum(expo, axis=-1, keepdims=True))).astype(jnp.bfloat16)
        mixed = mixed + jnp.dot(probs, vh, preferred_element_type=jnp.float32)
    mixed = mixed.astype(jnp.bfloat16)
    fine = (x + jnp.dot(mixed, wo_ref[...], preferred_element_type=jnp.float32)).astype(jnp.bfloat16)
    row_live = lax.broadcasted_iota(jnp.int32, (BALL, 1), 0) < count
    masked_ref[...] = jnp.where(row_live, fine, jnp.zeros((), jnp.bfloat16))
    hidden = jnp.dot(_norm(fine.astype(jnp.float32)), w1_ref[...], preferred_element_type=jnp.float32)
    hidden = jax.nn.gelu(hidden, approximate=True).astype(jnp.bfloat16)
    refined_ref[...] = fine.astype(jnp.float32) + jnp.dot(hidden, w2_ref[...], preferred_element_type=jnp.float32)


def ball_block(tree_rows, ball_counts, ball_proj, ball_out, mlp_in, mlp_out):
    rows, feature = tree_rows.shape
    ff = mlp_in.shape[1]
    balls = rows // BALL
    const2 = lambda i, c: (0, 0)
    return pl.pallas_call(
        _ball_kernel,
        out_shape=(jax.ShapeDtypeStruct((rows, feature), jnp.bfloat16),
                   jax.ShapeDtypeStruct((rows, feature), jnp.float32)),
        grid_spec=pltpu.PrefetchScalarGridSpec(
            num_scalar_prefetch=1, grid=(balls,),
            in_specs=[pl.BlockSpec((BALL, feature), lambda i, c: (i, 0)),
                      pl.BlockSpec((3, feature, feature), lambda i, c: (0, 0, 0)),
                      pl.BlockSpec((feature, feature), const2),
                      pl.BlockSpec((feature, ff), const2),
                      pl.BlockSpec((ff, feature), const2)],
            out_specs=[pl.BlockSpec((BALL, feature), lambda i, c: (i, 0)),
                       pl.BlockSpec((BALL, feature), lambda i, c: (i, 0))]),
        compiler_params=pltpu.CompilerParams(dimension_semantics=("arbitrary",)),
    )(ball_counts, tree_rows, ball_proj, ball_out, mlp_in, mlp_out)


def gather_all(shard, axis, order):
    gathered = shard
    for apart in order:
        gathered = jnp.concatenate([gathered, partner(gathered, axis, apart)], axis=0)
    return gathered


def partner(shard, axis, apart):
    return lax.ppermute(shard, axis, [(i, i ^ 1 << apart) for i in range(lax.axis_size(axis))])


def normalize(inputs):
    inputs = inputs.astype(jnp.float32)
    center = inputs - jnp.mean(inputs, axis=-1, keepdims=True)
    spread = jnp.mean(center * center, axis=-1, keepdims=True)
    return (center * lax.rsqrt(spread + EPSILON)).astype(jnp.bfloat16)


def project(inputs, weight):
    return jnp.dot(inputs, weight, preferred_element_type=jnp.float32).astype(jnp.bfloat16)


def attend(queries, key_rows, value_rows, valid, head_count):
    groups, q_rows, feature = queries.shape
    k_rows = key_rows.shape[1]
    head_size = feature // head_count
    q_heads = queries.reshape(groups, q_rows, head_count, head_size)
    k_heads = key_rows.reshape(groups, k_rows, head_count, head_size)
    v_heads = value_rows.reshape(groups, k_rows, head_count, head_size)
    scores = jnp.einsum(
        "bqhd,bkhd->bhqk", q_heads, k_heads, preferred_element_type=jnp.float32
    ) / math.sqrt(head_size)
    if valid is not None:
        scores = jnp.where(valid[:, None, None, :], scores, -1e30)
    row_max = jnp.max(scores, axis=-1, keepdims=True)
    expo = jnp.exp(scores - row_max)
    attn_probs = (expo / jnp.sum(expo, axis=-1, keepdims=True)).astype(jnp.bfloat16)
    mixed = jnp.einsum("bhqk,bkhd->bqhd", attn_probs, v_heads, preferred_element_type=jnp.float32)
    return mixed.reshape(groups, q_rows, feature).astype(jnp.bfloat16)


def coarse_qkv(coarse_state, weights):
    normed = normalize(coarse_state)
    return (project(normed, weights[0]), project(normed, weights[1]), project(normed, weights[2]))


def coarse_update(coarse_state, queries, key_rows, value_rows, out_weight):
    mixed = attend(queries, key_rows, value_rows, None, HEADS)
    return coarse_state + jnp.dot(mixed, out_weight, preferred_element_type=jnp.float32)


def local(
    points,
    tree_order,
    ball_counts,
    ball_proj,
    ball_out,
    pool_weight,
    coarse_proj,
    coarse_out,
    global_proj,
    global_out,
    unpool_weight,
    mlp_in,
    mlp_out,
):
    row_count, feature = points.shape
    offset = lax.axis_index("point") * row_count
    tree_rows = jnp.take(points, tree_order - offset, axis=0)
    live_mask = (jnp.arange(BALL, dtype=jnp.int32)[None, :] < ball_counts[:, None]).reshape(-1)
    masked, refined = ball_block(tree_rows, ball_counts, ball_proj, ball_out, mlp_in, mlp_out)
    pooled = jnp.dot(
        masked.reshape(row_count // POOL, POOL * feature),
        pool_weight,
        preferred_element_type=jnp.float32,
    )
    device_count = lax.axis_size("point")
    level_count = device_count.bit_length() - 1
    coarse_state = pooled[None]
    for level_index in range(level_count):
        queries, key_rows, value_rows = coarse_qkv(coarse_state, coarse_proj)
        received = partner(jnp.stack([key_rows, value_rows]), "point", level_index)
        coarse_state = coarse_update(
            coarse_state,
            queries,
            jnp.concatenate([key_rows, received[0]], axis=1),
            jnp.concatenate([value_rows, received[1]], axis=1),
            coarse_out,
        )
    queries, key_rows, value_rows = coarse_qkv(coarse_state, global_proj)
    both = gather_all(jnp.concatenate([key_rows[0], value_rows[0]], axis=1), "point", GATHER_ORDER)
    all_keys, all_values = both[None, :, :feature], both[None, :, feature:]
    mixed = attend(queries, all_keys, all_values, None, HEADS)
    summary = (
        coarse_state + jnp.dot(mixed, global_out, preferred_element_type=jnp.float32)
    ).astype(jnp.bfloat16)
    unpooled = jnp.dot(
        summary.reshape(-1, feature), unpool_weight, preferred_element_type=jnp.float32
    ).reshape(row_count, feature)
    total = refined + unpooled
    return jnp.where(live_mask[:, None], total, 0.0).astype(jnp.bfloat16)


def solution(mesh):
    placed = (
        P(("dp", "point"), None),
        P(("dp", "point")),
        P(("dp", "point")),
        P(),
        P(),
        P(),
        P(),
        P(),
        P(),
        P(),
        P(),
        P(),
        P(),
    )
    return jax.shard_map(
        local, mesh=mesh, in_specs=placed, out_specs=P(("dp", "point"), None), check_vma=False
    )
```

```python
import math

import jax
import jax.numpy as jnp
from jax import lax
from jax.experimental import pallas as pl
from jax.experimental.pallas import tpu as pltpu
from jax.sharding import PartitionSpec as P


HEADS = 8
BALL = 256
POOL = 64


EPSILON = 1e-05
GATHER_ORDER = (1, 4, 0, 2, 3)
MLP_CHUNK_ROWS = 1024


def _norm(x):
    center = x - jnp.mean(x, axis=-1, keepdims=True)
    spread = jnp.mean(center * center, axis=-1, keepdims=True)
    return (center * lax.rsqrt(spread + EPSILON)).astype(jnp.bfloat16)


def _ball_kernel(counts_ref, x_ref, proj_ref, wo_ref, masked_ref):
    count = counts_ref[pl.program_id(0)]
    x = x_ref[...].astype(jnp.float32)
    feature = x.shape[-1]
    head_size = feature // HEADS
    normed = _norm(x)
    q = jnp.dot(normed, proj_ref[0], preferred_element_type=jnp.float32).astype(jnp.bfloat16)
    k = jnp.dot(normed, proj_ref[1], preferred_element_type=jnp.float32).astype(jnp.bfloat16)
    v = jnp.dot(normed, proj_ref[2], preferred_element_type=jnp.float32).astype(jnp.bfloat16)
    key_live = lax.broadcasted_iota(jnp.int32, (1, BALL), 1) < count
    lane = lax.broadcasted_iota(jnp.int32, (1, feature), 1)
    scale = 1.0 / math.sqrt(head_size)
    mixed = jnp.zeros((BALL, feature), jnp.float32)
    for h in range(HEADS):
        in_head = (lane >= h * head_size) & (lane < (h + 1) * head_size)
        qh = jnp.where(in_head, q, jnp.zeros((), jnp.bfloat16))
        vh = jnp.where(in_head, v, jnp.zeros((), jnp.bfloat16))
        scores = lax.dot_general(qh, k, (((1,), (1,)), ((), ())), preferred_element_type=jnp.float32) * scale
        scores = jnp.where(key_live, scores, -1e30)
        row_max = jnp.max(scores, axis=-1, keepdims=True)
        expo = jnp.exp(scores - row_max)
        probs = (expo * (1.0 / jnp.sum(expo, axis=-1, keepdims=True))).astype(jnp.bfloat16)
        mixed = mixed + jnp.dot(probs, vh, preferred_element_type=jnp.float32)
    mixed = mixed.astype(jnp.bfloat16)
    fine = (x + jnp.dot(mixed, wo_ref[...], preferred_element_type=jnp.float32)).astype(jnp.bfloat16)
    row_live = lax.broadcasted_iota(jnp.int32, (BALL, 1), 0) < count
    masked_ref[...] = jnp.where(row_live, fine, jnp.zeros((), jnp.bfloat16))


def ball_block(tree_rows, ball_counts, ball_proj, ball_out):
    rows, feature = tree_rows.shape
    balls = rows // BALL
    return pl.pallas_call(
        _ball_kernel,
        out_shape=jax.ShapeDtypeStruct((rows, feature), jnp.bfloat16),
        grid_spec=pltpu.PrefetchScalarGridSpec(
            num_scalar_prefetch=1, grid=(balls,),
            in_specs=[pl.BlockSpec((BALL, feature), lambda i, c: (i, 0)),
                      pl.BlockSpec((3, feature, feature), lambda i, c: (0, 0, 0)),
                      pl.BlockSpec((feature, feature), lambda i, c: (0, 0))],
            out_specs=pl.BlockSpec((BALL, feature), lambda i, c: (i, 0))),
        compiler_params=pltpu.CompilerParams(dimension_semantics=("arbitrary",)),
    )(ball_counts, tree_rows, ball_proj, ball_out)


def _mlp_kernel(fine_ref, w1_ref, w2_ref, refined_ref):
    fine = fine_ref[...]
    hidden = jnp.dot(_norm(fine.astype(jnp.float32)), w1_ref[...], preferred_element_type=jnp.float32)
    hidden = jax.nn.gelu(hidden, approximate=True).astype(jnp.bfloat16)
    refined_ref[...] = fine.astype(jnp.float32) + jnp.dot(hidden, w2_ref[...], preferred_element_type=jnp.float32)


def mlp_block(fine, mlp_in, mlp_out):
    rows, feature = fine.shape
    ff = mlp_in.shape[1]
    return pl.pallas_call(
        _mlp_kernel,
        out_shape=jax.ShapeDtypeStruct((rows, feature), jnp.float32),
        grid=(rows // BALL,),
        in_specs=[pl.BlockSpec((BALL, feature), lambda i: (i, 0)),
                  pl.BlockSpec((feature, ff), lambda i: (0, 0)),
                  pl.BlockSpec((ff, feature), lambda i: (0, 0))],
        out_specs=pl.BlockSpec((BALL, feature), lambda i: (i, 0)),
        compiler_params=pltpu.CompilerParams(dimension_semantics=("arbitrary",)),
    )(fine, mlp_in, mlp_out)


def gather_all(shard, axis, order):
    gathered = shard
    for apart in order:
        received = partner(gathered, axis, apart)
        gathered = jnp.concatenate([gathered, received], axis=0)
    return gathered


def partner(shard, axis, apart):
    return lax.ppermute(shard, axis, [(i, i ^ 1 << apart) for i in range(lax.axis_size(axis))])


def normalize(inputs):
    inputs = inputs.astype(jnp.float32)
    center = inputs - jnp.mean(inputs, axis=-1, keepdims=True)
    spread = jnp.mean(center * center, axis=-1, keepdims=True)
    return (center * lax.rsqrt(spread + EPSILON)).astype(jnp.bfloat16)


def project(inputs, weight):
    return jnp.dot(inputs, weight, preferred_element_type=jnp.float32).astype(jnp.bfloat16)


def attend(queries, key_rows, value_rows, valid, head_count):
    groups, q_rows, feature = queries.shape
    k_rows = key_rows.shape[1]
    head_size = feature // head_count
    q_heads = queries.reshape(groups, q_rows, head_count, head_size)
    k_heads = key_rows.reshape(groups, k_rows, head_count, head_size)
    v_heads = value_rows.reshape(groups, k_rows, head_count, head_size)
    scores = jnp.einsum(
        "bqhd,bkhd->bhqk", q_heads, k_heads, preferred_element_type=jnp.float32
    ) / math.sqrt(head_size)
    if valid is not None:
        scores = jnp.where(valid[:, None, None, :], scores, -1e30)
    row_max = jnp.max(scores, axis=-1, keepdims=True)
    expo = jnp.exp(scores - row_max)
    attn_probs = (expo / jnp.sum(expo, axis=-1, keepdims=True)).astype(jnp.bfloat16)
    mixed = jnp.einsum("bhqk,bkhd->bqhd", attn_probs, v_heads, preferred_element_type=jnp.float32)
    return mixed.reshape(groups, q_rows, feature).astype(jnp.bfloat16)


def coarse_qkv(coarse_state, weights):
    normed = normalize(coarse_state)
    return (project(normed, weights[0]), project(normed, weights[1]), project(normed, weights[2]))


def coarse_update(coarse_state, queries, key_rows, value_rows, out_weight):
    mixed = attend(queries, key_rows, value_rows, None, HEADS)
    return coarse_state + jnp.dot(mixed, out_weight, preferred_element_type=jnp.float32)


def local_body(
    points,
    tree_order,
    ball_counts,
    ball_proj,
    ball_out,
    pool_weight,
    coarse_proj,
    coarse_out,
    global_proj,
    global_out,
    unpool_weight,
    mlp_in,
    mlp_out,
):
    row_count, feature = points.shape
    offset = lax.axis_index("point") * row_count
    tree_rows = jnp.take(points, tree_order - offset, axis=0)
    live_mask = (jnp.arange(BALL, dtype=jnp.int32)[None, :] < ball_counts[:, None]).reshape(-1)
    masked = ball_block(tree_rows, ball_counts, ball_proj, ball_out)
    chunk = MLP_CHUNK_ROWS
    refined_parts = []
    for start in range(0, row_count, chunk):
        refined_parts.append(mlp_block(masked[start:start + chunk], mlp_in, mlp_out))
    pooled = jnp.dot(
        masked.reshape(row_count // POOL, POOL * feature),
        pool_weight,
        preferred_element_type=jnp.float32,
    )
    device_count = lax.axis_size("point")
    level_count = device_count.bit_length() - 1
    coarse_state = pooled[None]
    for level_index in range(level_count):
        queries, key_rows, value_rows = coarse_qkv(coarse_state, coarse_proj)
        received = partner(jnp.stack([key_rows, value_rows]), "point", level_index)
        coarse_state = coarse_update(
            coarse_state,
            queries,
            jnp.concatenate([key_rows, received[0]], axis=1),
            jnp.concatenate([value_rows, received[1]], axis=1),
            coarse_out,
        )
    normed = normalize(coarse_state)
    queries = project(normed, global_proj[0])
    everyone = gather_all(coarse_state[0].astype(jnp.bfloat16), "point", GATHER_ORDER)[None]
    normed_all = normalize(everyone)
    all_keys = project(normed_all, global_proj[1])
    all_values = project(normed_all, global_proj[2])
    mixed = attend(queries, all_keys, all_values, None, HEADS)
    summary = (
        coarse_state + jnp.dot(mixed, global_out, preferred_element_type=jnp.float32)
    ).astype(jnp.bfloat16)
    unpooled = jnp.dot(
        summary.reshape(-1, feature), unpool_weight, preferred_element_type=jnp.float32
    ).reshape(row_count, feature)
    total = jnp.concatenate(refined_parts, axis=0) + unpooled
    return jnp.where(live_mask[:, None], total, 0.0).astype(jnp.bfloat16)


def solution(mesh):
    placed = (
        P(("dp", "point"), None),
        P(("dp", "point")),
        P(("dp", "point")),
        P(),
        P(),
        P(),
        P(),
        P(),
        P(),
        P(),
        P(),
        P(),
        P(),
    )
    return jax.shard_map(local_body, mesh=mesh, in_specs=placed, out_specs=P(("dp", "point"), None), check_vma=False)
```

```python
import math

import jax
import jax.numpy as jnp
from jax import lax
from jax.experimental import pallas as pl
from jax.experimental.pallas import tpu as pltpu
from jax.sharding import PartitionSpec as P


HEADS = 8
BALL = 256
POOL = 64


EPSILON = 1e-05
GATHER_ORDER = (1, 4, 0, 2, 3)
MLP_CHUNK_ROWS = 1024


def _norm(x):
    center = x - jnp.mean(x, axis=-1, keepdims=True)
    spread = jnp.mean(center * center, axis=-1, keepdims=True)
    return (center * lax.rsqrt(spread + EPSILON)).astype(jnp.bfloat16)


def _ball_kernel(counts_ref, x_ref, proj_ref, wo_ref, masked_ref):
    count = counts_ref[pl.program_id(0)]
    x = x_ref[...].astype(jnp.float32)
    feature = x.shape[-1]
    head_size = feature // HEADS
    normed = _norm(x)
    q = jnp.dot(normed, proj_ref[0], preferred_element_type=jnp.float32).astype(jnp.bfloat16)
    k = jnp.dot(normed, proj_ref[1], preferred_element_type=jnp.float32).astype(jnp.bfloat16)
    v = jnp.dot(normed, proj_ref[2], preferred_element_type=jnp.float32).astype(jnp.bfloat16)
    k_t = k.T
    key_live = lax.broadcasted_iota(jnp.int32, (1, BALL), 1) < count
    lane = lax.broadcasted_iota(jnp.int32, (1, feature), 1)
    scale = 1.0 / math.sqrt(head_size)
    mixed = jnp.zeros((BALL, feature), jnp.float32)
    for h in range(HEADS):
        in_head = (lane >= h * head_size) & (lane < (h + 1) * head_size)
        qh = jnp.where(in_head, q, jnp.zeros((), jnp.bfloat16))
        vh = jnp.where(in_head, v, jnp.zeros((), jnp.bfloat16))
        scores = jnp.dot(qh, k_t, preferred_element_type=jnp.float32) * scale
        scores = jnp.where(key_live, scores, -1e30)
        row_max = jnp.max(scores, axis=-1, keepdims=True)
        expo = jnp.exp(scores - row_max)
        probs = (expo * (1.0 / jnp.sum(expo, axis=-1, keepdims=True))).astype(jnp.bfloat16)
        mixed = mixed + jnp.dot(probs, vh, preferred_element_type=jnp.float32)
    mixed = mixed.astype(jnp.bfloat16)
    fine = (x + jnp.dot(mixed, wo_ref[...], preferred_element_type=jnp.float32)).astype(jnp.bfloat16)
    row_live = lax.broadcasted_iota(jnp.int32, (BALL, 1), 0) < count
    masked_ref[...] = jnp.where(row_live, fine, jnp.zeros((), jnp.bfloat16))


def ball_block(tree_rows, ball_counts, ball_proj, ball_out):
    rows, feature = tree_rows.shape
    balls = rows // BALL
    return pl.pallas_call(
        _ball_kernel,
        out_shape=jax.ShapeDtypeStruct((rows, feature), jnp.bfloat16),
        grid_spec=pltpu.PrefetchScalarGridSpec(
            num_scalar_prefetch=1, grid=(balls,),
            in_specs=[pl.BlockSpec((BALL, feature), lambda i, c: (i, 0)),
                      pl.BlockSpec((3, feature, feature), lambda i, c: (0, 0, 0)),
                      pl.BlockSpec((feature, feature), lambda i, c: (0, 0))],
            out_specs=pl.BlockSpec((BALL, feature), lambda i, c: (i, 0))),
        compiler_params=pltpu.CompilerParams(dimension_semantics=("arbitrary",)),
    )(ball_counts, tree_rows, ball_proj, ball_out)


def _mlp_kernel(fine_ref, w1_ref, w2_ref, refined_ref):
    fine = fine_ref[...]
    hidden = jnp.dot(_norm(fine.astype(jnp.float32)), w1_ref[...], preferred_element_type=jnp.float32)
    hidden = jax.nn.gelu(hidden, approximate=True).astype(jnp.bfloat16)
    refined_ref[...] = fine.astype(jnp.float32) + jnp.dot(hidden, w2_ref[...], preferred_element_type=jnp.float32)


def mlp_block(fine, refined, first_block, block_count, mlp_in, mlp_out):
    rows, feature = fine.shape
    ff = mlp_in.shape[1]
    in_specs = [pl.BlockSpec((BALL, feature), lambda i: (first_block + i, 0)),
                pl.BlockSpec((feature, ff), lambda i: (0, 0)),
                pl.BlockSpec((ff, feature), lambda i: (0, 0))]
    operands = [fine, mlp_in, mlp_out]
    aliases = {}
    if refined is not None:
        in_specs.append(pl.BlockSpec(memory_space=pl.ANY))
        operands.append(refined)
        aliases = {3: 0}
    kernel = _mlp_kernel if refined is None else (lambda f, w1, w2, _, out: _mlp_kernel(f, w1, w2, out))
    return pl.pallas_call(
        kernel,
        out_shape=jax.ShapeDtypeStruct((rows, feature), jnp.float32),
        grid=(block_count,),
        in_specs=in_specs,
        out_specs=pl.BlockSpec((BALL, feature), lambda i: (first_block + i, 0)),
        input_output_aliases=aliases,
        compiler_params=pltpu.CompilerParams(dimension_semantics=("arbitrary",)),
    )(*operands)


def _final_kernel(counts_ref, refined_ref, unpooled_ref, out_ref):
    slots, tokens, _ = unpooled_ref.shape
    first_token = pl.program_id(0) * tokens
    slot = lax.broadcasted_iota(jnp.int32, (slots, 1), 0)
    for token in range(tokens):
        ball = (first_token + token) * slots // BALL
        start_in_ball = ((first_token + token) * slots) % BALL
        live = start_in_ball + slot < counts_ref[ball]
        rows = pl.ds(token * slots, slots)
        total = refined_ref[rows, :] + unpooled_ref[:, token, :]
        out_ref[rows, :] = jnp.where(live, total, 0.0).astype(out_ref.dtype)


def final_block(ball_counts, refined, unpooled):
    rows, feature = refined.shape
    slots, tokens, _ = unpooled.shape
    per_step = 8
    return pl.pallas_call(
        _final_kernel,
        out_shape=jax.ShapeDtypeStruct((rows, feature), jnp.bfloat16),
        grid_spec=pltpu.PrefetchScalarGridSpec(
            num_scalar_prefetch=1, grid=(tokens // per_step,),
            in_specs=[pl.BlockSpec((per_step * slots, feature), lambda i, c: (i, 0)),
                      pl.BlockSpec((slots, per_step, feature), lambda i, c: (0, i, 0))],
            out_specs=pl.BlockSpec((per_step * slots, feature), lambda i, c: (i, 0))),
        compiler_params=pltpu.CompilerParams(dimension_semantics=("arbitrary",)),
    )(ball_counts, refined, unpooled)


def gather_all(shard, axis, order):
    gathered = shard
    for apart in order:
        received = partner(gathered, axis, apart)
        gathered = jnp.concatenate([gathered, received], axis=0)
    return gathered


def partner(shard, axis, apart):
    return lax.ppermute(shard, axis, [(i, i ^ 1 << apart) for i in range(lax.axis_size(axis))])


def normalize(inputs):
    inputs = inputs.astype(jnp.float32)
    center = inputs - jnp.mean(inputs, axis=-1, keepdims=True)
    spread = jnp.mean(center * center, axis=-1, keepdims=True)
    return (center * lax.rsqrt(spread + EPSILON)).astype(jnp.bfloat16)


def project(inputs, weight):
    return jnp.dot(inputs, weight, preferred_element_type=jnp.float32).astype(jnp.bfloat16)


def attend(queries, key_rows, value_rows, valid, head_count):
    groups, q_rows, feature = queries.shape
    k_rows = key_rows.shape[1]
    head_size = feature // head_count
    q_heads = queries.reshape(groups, q_rows, head_count, head_size)
    k_heads = key_rows.reshape(groups, k_rows, head_count, head_size)
    v_heads = value_rows.reshape(groups, k_rows, head_count, head_size)
    scores = jnp.einsum(
        "bqhd,bkhd->bhqk", q_heads, k_heads, preferred_element_type=jnp.float32
    ) / math.sqrt(head_size)
    if valid is not None:
        scores = jnp.where(valid[:, None, None, :], scores, -1e30)
    row_max = jnp.max(scores, axis=-1, keepdims=True)
    expo = jnp.exp(scores - row_max)
    attn_probs = (expo / jnp.sum(expo, axis=-1, keepdims=True)).astype(jnp.bfloat16)
    mixed = jnp.einsum("bhqk,bkhd->bqhd", attn_probs, v_heads, preferred_element_type=jnp.float32)
    return mixed.reshape(groups, q_rows, feature).astype(jnp.bfloat16)


def coarse_qkv(coarse_state, weights):
    normed = normalize(coarse_state)
    return (project(normed, weights[0]), project(normed, weights[1]), project(normed, weights[2]))


def coarse_update(coarse_state, queries, key_rows, value_rows, out_weight):
    mixed = attend(queries, key_rows, value_rows, None, HEADS)
    return coarse_state + jnp.dot(mixed, out_weight, preferred_element_type=jnp.float32)


def local_body(
    points,
    tree_order,
    ball_counts,
    ball_proj,
    ball_out,
    pool_weight,
    coarse_proj,
    coarse_out,
    global_proj,
    global_out,
    unpool_weight,
    mlp_in,
    mlp_out,
):
    row_count, feature = points.shape
    offset = lax.axis_index("point") * row_count
    tree_rows = jnp.take(points, tree_order - offset, axis=0)
    live_mask = (jnp.arange(BALL, dtype=jnp.int32)[None, :] < ball_counts[:, None]).reshape(-1)
    masked = ball_block(tree_rows, ball_counts, ball_proj, ball_out)
    chunk = MLP_CHUNK_ROWS
    refined = None
    for start in range(0, row_count, chunk):
        refined = mlp_block(masked, refined, start // BALL, chunk // BALL, mlp_in, mlp_out)
    pooled = jnp.einsum(
        "rjd,jde->re",
        masked.reshape(row_count // POOL, POOL, feature),
        pool_weight.reshape(POOL, feature, feature),
        preferred_element_type=jnp.float32,
    )
    device_count = lax.axis_size("point")
    level_count = device_count.bit_length() - 1
    coarse_state = pooled[None]
    for level_index in range(level_count):
        queries, key_rows, value_rows = coarse_qkv(coarse_state, coarse_proj)
        received = partner(jnp.stack([key_rows, value_rows]), "point", level_index)
        coarse_state = coarse_update(
            coarse_state,
            queries,
            jnp.concatenate([key_rows, received[0]], axis=1),
            jnp.concatenate([value_rows, received[1]], axis=1),
            coarse_out,
        )
    normed = normalize(coarse_state)
    queries = project(normed, global_proj[0])
    everyone = gather_all(coarse_state[0].astype(jnp.bfloat16), "point", GATHER_ORDER)[None]
    normed_all = normalize(everyone)
    all_keys = project(normed_all, global_proj[1])
    all_values = project(normed_all, global_proj[2])
    mixed = attend(queries, all_keys, all_values, None, HEADS)
    summary = (
        coarse_state + jnp.dot(mixed, global_out, preferred_element_type=jnp.float32)
    ).astype(jnp.bfloat16)
    unpooled = jnp.einsum(
        "rd,dje->jre",
        summary.reshape(-1, feature),
        unpool_weight.reshape(feature, POOL, feature),
        preferred_element_type=jnp.float32,
    )
    return final_block(ball_counts, refined, unpooled)


def solution(mesh):
    placed = (
        P(("dp", "point"), None),
        P(("dp", "point")),
        P(("dp", "point")),
        P(),
        P(),
        P(),
        P(),
        P(),
        P(),
        P(),
        P(),
        P(),
        P(),
    )
    return jax.shard_map(local_body, mesh=mesh, in_specs=placed, out_specs=P(("dp", "point"), None), check_vma=False)
```

```python
import math

import jax
import jax.numpy as jnp
from jax import lax
from jax.experimental import pallas as pl
from jax.experimental.pallas import tpu as pltpu
from jax.sharding import PartitionSpec as P


HEADS = 8
BALL = 256
POOL = 64


EPSILON = 1e-05
GATHER_ORDER = (1, 4, 0, 2, 3)
MLP_CHUNK_ROWS = 1024


def _norm(x):
    center = x - jnp.mean(x, axis=-1, keepdims=True)
    spread = jnp.mean(center * center, axis=-1, keepdims=True)
    return (center * lax.rsqrt(spread + EPSILON)).astype(jnp.bfloat16)


def _ball_kernel(counts_ref, x_ref, proj_ref, wo_ref, masked_ref):
    count = counts_ref[pl.program_id(0)]
    x = x_ref[...].astype(jnp.float32)
    feature = x.shape[-1]
    head_size = feature // HEADS
    normed = _norm(x)
    q = jnp.dot(normed, proj_ref[0], preferred_element_type=jnp.float32).astype(jnp.bfloat16)
    k = jnp.dot(normed, proj_ref[1], preferred_element_type=jnp.float32).astype(jnp.bfloat16)
    v = jnp.dot(normed, proj_ref[2], preferred_element_type=jnp.float32).astype(jnp.bfloat16)
    k_t = k.T
    key_live = lax.broadcasted_iota(jnp.int32, (1, BALL), 1) < count
    lane = lax.broadcasted_iota(jnp.int32, (1, feature), 1)
    scale = 1.0 / math.sqrt(head_size)
    mixed = jnp.zeros((BALL, feature), jnp.float32)
    for h in range(HEADS):
        in_head = (lane >= h * head_size) & (lane < (h + 1) * head_size)
        qh = jnp.where(in_head, q, jnp.zeros((), jnp.bfloat16))
        vh = jnp.where(in_head, v, jnp.zeros((), jnp.bfloat16))
        scores = jnp.dot(qh, k_t, preferred_element_type=jnp.float32) * scale
        scores = jnp.where(key_live, scores, -1e30)
        row_max = jnp.max(scores, axis=-1, keepdims=True)
        expo = jnp.exp(scores - row_max)
        probs = (expo * (1.0 / jnp.sum(expo, axis=-1, keepdims=True))).astype(jnp.bfloat16)
        mixed = mixed + jnp.dot(probs, vh, preferred_element_type=jnp.float32)
    mixed = mixed.astype(jnp.bfloat16)
    fine = (x + jnp.dot(mixed, wo_ref[...], preferred_element_type=jnp.float32)).astype(jnp.bfloat16)
    row_live = lax.broadcasted_iota(jnp.int32, (BALL, 1), 0) < count
    masked_ref[...] = jnp.where(row_live, fine, jnp.zeros((), jnp.bfloat16))


def ball_block(tree_rows, ball_counts, ball_proj, ball_out):
    rows, feature = tree_rows.shape
    balls = rows // BALL
    return pl.pallas_call(
        _ball_kernel,
        out_shape=jax.ShapeDtypeStruct((rows, feature), jnp.bfloat16),
        grid_spec=pltpu.PrefetchScalarGridSpec(
            num_scalar_prefetch=1, grid=(balls,),
            in_specs=[pl.BlockSpec((BALL, feature), lambda i, c: (i, 0)),
                      pl.BlockSpec((3, feature, feature), lambda i, c: (0, 0, 0)),
                      pl.BlockSpec((feature, feature), lambda i, c: (0, 0))],
            out_specs=pl.BlockSpec((BALL, feature), lambda i, c: (i, 0))),
        compiler_params=pltpu.CompilerParams(dimension_semantics=("arbitrary",)),
    )(ball_counts, tree_rows, ball_proj, ball_out)


def _mlp_kernel(fine_ref, w1_ref, w2_ref, refined_ref):
    fine = fine_ref[...]
    hidden = jnp.dot(_norm(fine.astype(jnp.float32)), w1_ref[...], preferred_element_type=jnp.float32)
    hidden = jax.nn.gelu(hidden, approximate=True).astype(jnp.bfloat16)
    refined_ref[...] = fine.astype(jnp.float32) + jnp.dot(hidden, w2_ref[...], preferred_element_type=jnp.float32)


def mlp_block(fine, refined, first_block, block_count, mlp_in, mlp_out):
    rows, feature = fine.shape
    ff = mlp_in.shape[1]
    in_specs = [pl.BlockSpec((BALL, feature), lambda i: (first_block + i, 0)),
                pl.BlockSpec((feature, ff), lambda i: (0, 0)),
                pl.BlockSpec((ff, feature), lambda i: (0, 0))]
    operands = [fine, mlp_in, mlp_out]
    aliases = {}
    if refined is not None:
        in_specs.append(pl.BlockSpec(memory_space=pl.ANY))
        operands.append(refined)
        aliases = {3: 0}
    kernel = _mlp_kernel if refined is None else (lambda f, w1, w2, _, out: _mlp_kernel(f, w1, w2, out))
    return pl.pallas_call(
        kernel,
        out_shape=jax.ShapeDtypeStruct((rows, feature), jnp.float32),
        grid=(block_count,),
        in_specs=in_specs,
        out_specs=pl.BlockSpec((BALL, feature), lambda i: (first_block + i, 0)),
        input_output_aliases=aliases,
        compiler_params=pltpu.CompilerParams(dimension_semantics=("arbitrary",)),
    )(*operands)


def _final_kernel(counts_ref, refined_ref, unpooled_hbm, out_ref, staged, arrived):
    step = pl.program_id(0)
    tokens, slots, _ = staged.shape[1:]

    def fetch(at, into):
        for token in range(tokens):
            pltpu.make_async_copy(
                unpooled_hbm.at[:, at * tokens + token, :], staged.at[into, token], arrived.at[into]
            ).start()

    @pl.when(step == 0)
    def _():
        fetch(0, 0)

    @pl.when(step + 1 < pl.num_programs(0))
    def _():
        fetch(step + 1, (step + 1) % 2)

    current = step % 2
    pltpu.make_async_copy(
        unpooled_hbm.at[pl.ds(0, tokens), pl.ds(0, slots), :], staged.at[current], arrived.at[current]
    ).wait()
    slot = lax.broadcasted_iota(jnp.int32, (slots, 1), 0)
    for token in range(tokens):
        first_row = (step * tokens + token) * slots
        live = first_row % BALL + slot < counts_ref[first_row // BALL]
        rows = pl.ds(token * slots, slots)
        total = refined_ref[rows, :] + staged[current, token]
        out_ref[rows, :] = jnp.where(live, total, 0.0).astype(out_ref.dtype)


def final_block(ball_counts, refined, unpooled):
    rows, feature = refined.shape
    slots, tokens, _ = unpooled.shape
    per_step = 8
    return pl.pallas_call(
        _final_kernel,
        out_shape=jax.ShapeDtypeStruct((rows, feature), jnp.bfloat16),
        grid_spec=pltpu.PrefetchScalarGridSpec(
            num_scalar_prefetch=1, grid=(tokens // per_step,),
            in_specs=[pl.BlockSpec((per_step * slots, feature), lambda i, c: (i, 0)),
                      pl.BlockSpec(memory_space=pl.ANY)],
            out_specs=pl.BlockSpec((per_step * slots, feature), lambda i, c: (i, 0)),
            scratch_shapes=[pltpu.VMEM((2, per_step, slots, feature), jnp.float32),
                            pltpu.SemaphoreType.DMA((2,))]),
        compiler_params=pltpu.CompilerParams(dimension_semantics=("arbitrary",)),
    )(ball_counts, refined, unpooled)


def gather_all(shard, axis, order):
    gathered = shard
    for apart in order:
        received = partner(gathered, axis, apart)
        gathered = jnp.concatenate([gathered, received], axis=0)
    return gathered


def partner(shard, axis, apart):
    return lax.ppermute(shard, axis, [(i, i ^ 1 << apart) for i in range(lax.axis_size(axis))])


def normalize(inputs):
    inputs = inputs.astype(jnp.float32)
    center = inputs - jnp.mean(inputs, axis=-1, keepdims=True)
    spread = jnp.mean(center * center, axis=-1, keepdims=True)
    return (center * lax.rsqrt(spread + EPSILON)).astype(jnp.bfloat16)


def project(inputs, weight):
    return jnp.dot(inputs, weight, preferred_element_type=jnp.float32).astype(jnp.bfloat16)


def attend(queries, key_rows, value_rows, valid, head_count):
    groups, q_rows, feature = queries.shape
    k_rows = key_rows.shape[1]
    head_size = feature // head_count
    q_heads = queries.reshape(groups, q_rows, head_count, head_size)
    k_heads = key_rows.reshape(groups, k_rows, head_count, head_size)
    v_heads = value_rows.reshape(groups, k_rows, head_count, head_size)
    scores = jnp.einsum(
        "bqhd,bkhd->bhqk", q_heads, k_heads, preferred_element_type=jnp.float32
    ) / math.sqrt(head_size)
    if valid is not None:
        scores = jnp.where(valid[:, None, None, :], scores, -1e30)
    row_max = jnp.max(scores, axis=-1, keepdims=True)
    expo = jnp.exp(scores - row_max)
    attn_probs = (expo / jnp.sum(expo, axis=-1, keepdims=True)).astype(jnp.bfloat16)
    mixed = jnp.einsum("bhqk,bkhd->bqhd", attn_probs, v_heads, preferred_element_type=jnp.float32)
    return mixed.reshape(groups, q_rows, feature).astype(jnp.bfloat16)


def coarse_qkv(coarse_state, weights):
    normed = normalize(coarse_state)
    return (project(normed, weights[0]), project(normed, weights[1]), project(normed, weights[2]))


def coarse_update(coarse_state, queries, key_rows, value_rows, out_weight):
    mixed = attend(queries, key_rows, value_rows, None, HEADS)
    return coarse_state + jnp.dot(mixed, out_weight, preferred_element_type=jnp.float32)


def local_body(
    points,
    tree_order,
    ball_counts,
    ball_proj,
    ball_out,
    pool_weight,
    coarse_proj,
    coarse_out,
    global_proj,
    global_out,
    unpool_weight,
    mlp_in,
    mlp_out,
):
    row_count, feature = points.shape
    offset = lax.axis_index("point") * row_count
    tree_rows = points.at[tree_order - offset].get(mode="promise_in_bounds", unique_indices=True)
    live_mask = (jnp.arange(BALL, dtype=jnp.int32)[None, :] < ball_counts[:, None]).reshape(-1)
    masked = ball_block(tree_rows, ball_counts, ball_proj, ball_out)
    chunk = MLP_CHUNK_ROWS
    refined = None
    for start in range(0, row_count, chunk):
        refined = mlp_block(masked, refined, start // BALL, chunk // BALL, mlp_in, mlp_out)
    pooled = jnp.einsum(
        "rjd,jde->re",
        masked.reshape(row_count // POOL, POOL, feature),
        pool_weight.reshape(POOL, feature, feature),
        preferred_element_type=jnp.float32,
    )
    device_count = lax.axis_size("point")
    level_count = device_count.bit_length() - 1
    coarse_state = pooled[None]
    for level_index in range(level_count):
        queries, key_rows, value_rows = coarse_qkv(coarse_state, coarse_proj)
        received = partner(jnp.stack([key_rows, value_rows]), "point", level_index)
        coarse_state = coarse_update(
            coarse_state,
            queries,
            jnp.concatenate([key_rows, received[0]], axis=1),
            jnp.concatenate([value_rows, received[1]], axis=1),
            coarse_out,
        )
    normed = normalize(coarse_state)
    queries = project(normed, global_proj[0])
    everyone = gather_all(coarse_state[0].astype(jnp.bfloat16), "point", GATHER_ORDER)[None]
    normed_all = normalize(everyone)
    all_keys = project(normed_all, global_proj[1])
    all_values = project(normed_all, global_proj[2])
    mixed = attend(queries, all_keys, all_values, None, HEADS)
    summary = (
        coarse_state + jnp.dot(mixed, global_out, preferred_element_type=jnp.float32)
    ).astype(jnp.bfloat16)
    unpooled = jnp.einsum(
        "rd,dje->jre",
        summary.reshape(-1, feature),
        unpool_weight.reshape(feature, POOL, feature),
        preferred_element_type=jnp.float32,
    )
    return final_block(ball_counts, refined, unpooled)


def solution(mesh):
    placed = (
        P(("dp", "point"), None),
        P(("dp", "point")),
        P(("dp", "point")),
        P(),
        P(),
        P(),
        P(),
        P(),
        P(),
        P(),
        P(),
        P(),
        P(),
    )
    return jax.shard_map(local_body, mesh=mesh, in_specs=placed, out_specs=P(("dp", "point"), None), check_vma=False)
```

```python
import math

import jax
import jax.numpy as jnp
from jax import lax
from jax.experimental import pallas as pl
from jax.experimental.pallas import tpu as pltpu
from jax.sharding import PartitionSpec as P


HEADS = 8
BALL = 256
POOL = 64


EPSILON = 1e-05
GATHER_ORDER = (1, 4, 0, 2, 3)
MLP_CHUNK_ROWS = 1024
MLP_BLOCK_ROWS = 256
BALLS_PER_STEP = 2
FINAL_TOKENS_PER_STEP = 16
GLOBAL_UNROLL = 2


def _norm(x):
    center = x - jnp.mean(x, axis=-1, keepdims=True)
    spread = jnp.mean(center * center, axis=-1, keepdims=True)
    return (center * lax.rsqrt(spread + EPSILON)).astype(jnp.bfloat16)


def _ball_kernel(counts_ref, x_ref, proj_ref, wo_ref, masked_ref):
    rows, feature = x_ref.shape
    balls = rows // BALL
    first_ball = pl.program_id(0) * balls
    x = x_ref[...].astype(jnp.float32)
    head_size = feature // HEADS
    normed = _norm(x)
    q = jnp.dot(normed, proj_ref[0], preferred_element_type=jnp.float32).astype(jnp.bfloat16)
    k = jnp.dot(normed, proj_ref[1], preferred_element_type=jnp.float32).astype(jnp.bfloat16)
    v = jnp.dot(normed, proj_ref[2], preferred_element_type=jnp.float32).astype(jnp.bfloat16)
    lane = lax.broadcasted_iota(jnp.int32, (1, feature), 1)
    scale = 1.0 / math.sqrt(head_size)
    mixed_balls = []
    for ball in range(balls):
        count = counts_ref[first_ball + ball]
        own = slice(ball * BALL, (ball + 1) * BALL)
        q_ball, v_ball = q[own], v[own]
        k_t = k[own].T
        key_live = lax.broadcasted_iota(jnp.int32, (1, BALL), 1) < count

        def head(h, mixed):
            in_head = (lane >= h * head_size) & (lane < (h + 1) * head_size)
            qh = jnp.where(in_head, q_ball, jnp.zeros((), jnp.bfloat16))
            vh = jnp.where(in_head, v_ball, jnp.zeros((), jnp.bfloat16))
            scores = jnp.dot(qh, k_t, preferred_element_type=jnp.float32) * scale
            scores = jnp.where(key_live, scores, -1e30)
            row_max = jnp.max(scores, axis=-1, keepdims=True)
            expo = jnp.exp(scores - row_max)
            probs = (expo * (1.0 / jnp.sum(expo, axis=-1, keepdims=True))).astype(jnp.bfloat16)
            return mixed + jnp.dot(probs, vh, preferred_element_type=jnp.float32)

        mixed = lax.fori_loop(0, HEADS, head, jnp.zeros((BALL, feature), jnp.float32), unroll=True)
        mixed_balls.append(mixed.astype(jnp.bfloat16))
    mixed = jnp.concatenate(mixed_balls, axis=0) if balls > 1 else mixed_balls[0]
    fine = (x + jnp.dot(mixed, wo_ref[...], preferred_element_type=jnp.float32)).astype(jnp.bfloat16)
    row = lax.broadcasted_iota(jnp.int32, (rows, 1), 0)
    count_of_row = jnp.zeros((rows, 1), jnp.int32)
    for ball in range(balls):
        count_of_row = jnp.where(row // BALL == ball, counts_ref[first_ball + ball], count_of_row)
    masked_ref[...] = jnp.where(row % BALL < count_of_row, fine, jnp.zeros((), jnp.bfloat16))


def ball_block(tree_rows, ball_counts, ball_proj, ball_out):
    rows, feature = tree_rows.shape
    block = BALLS_PER_STEP * BALL
    return pl.pallas_call(
        _ball_kernel,
        out_shape=jax.ShapeDtypeStruct((rows, feature), jnp.bfloat16),
        grid_spec=pltpu.PrefetchScalarGridSpec(
            num_scalar_prefetch=1, grid=(rows // block,),
            in_specs=[pl.BlockSpec((block, feature), lambda i, c: (i, 0)),
                      pl.BlockSpec((3, feature, feature), lambda i, c: (0, 0, 0)),
                      pl.BlockSpec((feature, feature), lambda i, c: (0, 0))],
            out_specs=pl.BlockSpec((block, feature), lambda i, c: (i, 0))),
        compiler_params=pltpu.CompilerParams(dimension_semantics=("arbitrary",)),
    )(ball_counts, tree_rows, ball_proj, ball_out)


def _mlp_kernel(fine_ref, w1_ref, w2_ref, refined_ref):
    fine = fine_ref[...]
    hidden = jnp.dot(_norm(fine.astype(jnp.float32)), w1_ref[...], preferred_element_type=jnp.float32)
    hidden = jax.nn.gelu(hidden, approximate=True).astype(jnp.bfloat16)
    refined_ref[...] = fine.astype(jnp.float32) + jnp.dot(hidden, w2_ref[...], preferred_element_type=jnp.float32)


def mlp_block(fine, refined, first_block, block_count, mlp_in, mlp_out):
    rows, feature = fine.shape
    ff = mlp_in.shape[1]
    in_specs = [pl.BlockSpec((MLP_BLOCK_ROWS, feature), lambda i: (first_block + i, 0)),
                pl.BlockSpec((feature, ff), lambda i: (0, 0)),
                pl.BlockSpec((ff, feature), lambda i: (0, 0))]
    operands = [fine, mlp_in, mlp_out]
    aliases = {}
    if refined is not None:
        in_specs.append(pl.BlockSpec(memory_space=pl.ANY))
        operands.append(refined)
        aliases = {3: 0}
    kernel = _mlp_kernel if refined is None else (lambda f, w1, w2, _, out: _mlp_kernel(f, w1, w2, out))
    return pl.pallas_call(
        kernel,
        out_shape=jax.ShapeDtypeStruct((rows, feature), jnp.float32),
        grid=(block_count,),
        in_specs=in_specs,
        out_specs=pl.BlockSpec((MLP_BLOCK_ROWS, feature), lambda i: (first_block + i, 0)),
        input_output_aliases=aliases,
        compiler_params=pltpu.CompilerParams(dimension_semantics=("arbitrary",)),
    )(*operands)


def _final_kernel(counts_ref, refined_ref, unpooled_hbm, out_ref, staged, arrived):
    step = pl.program_id(0)
    tokens, slots, _ = staged.shape[1:]

    def fetch(at, into):
        for token in range(tokens):
            pltpu.make_async_copy(
                unpooled_hbm.at[:, at * tokens + token, :], staged.at[into, token], arrived.at[into]
            ).start()

    @pl.when(step == 0)
    def _():
        fetch(0, 0)

    @pl.when(step + 1 < pl.num_programs(0))
    def _():
        fetch(step + 1, (step + 1) % 2)

    current = step % 2
    pltpu.make_async_copy(
        unpooled_hbm.at[pl.ds(0, tokens), pl.ds(0, slots), :], staged.at[current], arrived.at[current]
    ).wait()
    slot = lax.broadcasted_iota(jnp.int32, (slots, 1), 0)
    for token in range(tokens):
        first_row = (step * tokens + token) * slots
        live = first_row % BALL + slot < counts_ref[first_row // BALL]
        rows = pl.ds(token * slots, slots)
        total = refined_ref[rows, :] + staged[current, token]
        out_ref[rows, :] = jnp.where(live, total, 0.0).astype(out_ref.dtype)


def final_block(ball_counts, refined, unpooled):
    rows, feature = refined.shape
    slots, tokens, _ = unpooled.shape
    per_step = FINAL_TOKENS_PER_STEP
    return pl.pallas_call(
        _final_kernel,
        out_shape=jax.ShapeDtypeStruct((rows, feature), jnp.bfloat16),
        grid_spec=pltpu.PrefetchScalarGridSpec(
            num_scalar_prefetch=1, grid=(tokens // per_step,),
            in_specs=[pl.BlockSpec((per_step * slots, feature), lambda i, c: (i, 0)),
                      pl.BlockSpec(memory_space=pl.ANY)],
            out_specs=pl.BlockSpec((per_step * slots, feature), lambda i, c: (i, 0)),
            scratch_shapes=[pltpu.VMEM((2, per_step, slots, feature), jnp.float32),
                            pltpu.SemaphoreType.DMA((2,))]),
        compiler_params=pltpu.CompilerParams(dimension_semantics=("arbitrary",)),
    )(ball_counts, refined, unpooled)


def _global_kernel(state_ref, everyone_ref, proj_ref, wo_ref, summary_ref):
    state = state_ref[...]
    feature = state.shape[-1]
    head_size = feature // HEADS
    q = jnp.dot(_norm(state), proj_ref[0], preferred_element_type=jnp.float32).astype(jnp.bfloat16)
    normed_all = _norm(everyone_ref[...].astype(jnp.float32))
    k_t = jnp.dot(normed_all, proj_ref[1], preferred_element_type=jnp.float32).astype(jnp.bfloat16).T
    v = jnp.dot(normed_all, proj_ref[2], preferred_element_type=jnp.float32).astype(jnp.bfloat16)
    lane = lax.broadcasted_iota(jnp.int32, (1, feature), 1)
    scale = 1.0 / math.sqrt(head_size)

    def head(h, mixed):
        in_head = (lane >= h * head_size) & (lane < (h + 1) * head_size)
        qh = jnp.where(in_head, q, jnp.zeros((), jnp.bfloat16))
        vh = jnp.where(in_head, v, jnp.zeros((), jnp.bfloat16))
        scores = jnp.dot(qh, k_t, preferred_element_type=jnp.float32) * scale
        row_max = jnp.max(scores, axis=-1, keepdims=True)
        expo = jnp.exp(scores - row_max)
        probs = (expo * (1.0 / jnp.sum(expo, axis=-1, keepdims=True))).astype(jnp.bfloat16)
        return mixed + jnp.dot(probs, vh, preferred_element_type=jnp.float32)

    mixed = lax.fori_loop(0, HEADS, head, jnp.zeros(state.shape, jnp.float32), unroll=GLOBAL_UNROLL).astype(jnp.bfloat16)
    summary_ref[...] = (state + jnp.dot(mixed, wo_ref[...], preferred_element_type=jnp.float32)).astype(
        summary_ref.dtype)


def global_block(state, everyone, global_proj, global_out):
    return pl.pallas_call(
        _global_kernel,
        out_shape=jax.ShapeDtypeStruct(state.shape, jnp.bfloat16),
    )(state, everyone, global_proj, global_out)


def gather_all(shard, axis, order):
    gathered = shard
    for apart in order:
        received = partner(gathered, axis, apart)
        gathered = jnp.concatenate([gathered, received], axis=0)
    return gathered


def partner(shard, axis, apart):
    return lax.ppermute(shard, axis, [(i, i ^ 1 << apart) for i in range(lax.axis_size(axis))])


def normalize(inputs):
    inputs = inputs.astype(jnp.float32)
    center = inputs - jnp.mean(inputs, axis=-1, keepdims=True)
    spread = jnp.mean(center * center, axis=-1, keepdims=True)
    return (center * lax.rsqrt(spread + EPSILON)).astype(jnp.bfloat16)


def project(inputs, weight):
    return jnp.dot(inputs, weight, preferred_element_type=jnp.float32).astype(jnp.bfloat16)


def attend(queries, key_rows, value_rows, valid, head_count):
    groups, q_rows, feature = queries.shape
    k_rows = key_rows.shape[1]
    head_size = feature // head_count
    q_heads = queries.reshape(groups, q_rows, head_count, head_size)
    k_heads = key_rows.reshape(groups, k_rows, head_count, head_size)
    v_heads = value_rows.reshape(groups, k_rows, head_count, head_size)
    scores = jnp.einsum(
        "bqhd,bkhd->bhqk", q_heads, k_heads, preferred_element_type=jnp.float32
    ) / math.sqrt(head_size)
    if valid is not None:
        scores = jnp.where(valid[:, None, None, :], scores, -1e30)
    row_max = jnp.max(scores, axis=-1, keepdims=True)
    expo = jnp.exp(scores - row_max)
    attn_probs = (expo / jnp.sum(expo, axis=-1, keepdims=True)).astype(jnp.bfloat16)
    mixed = jnp.einsum("bhqk,bkhd->bqhd", attn_probs, v_heads, preferred_element_type=jnp.float32)
    return mixed.reshape(groups, q_rows, feature).astype(jnp.bfloat16)


def coarse_qkv(coarse_state, weights):
    normed = normalize(coarse_state)
    return (project(normed, weights[0]), project(normed, weights[1]), project(normed, weights[2]))


def coarse_update(coarse_state, queries, key_rows, value_rows, out_weight):
    mixed = attend(queries, key_rows, value_rows, None, HEADS)
    return coarse_state + jnp.dot(mixed, out_weight, preferred_element_type=jnp.float32)


def local_body(
    points,
    tree_order,
    ball_counts,
    ball_proj,
    ball_out,
    pool_weight,
    coarse_proj,
    coarse_out,
    global_proj,
    global_out,
    unpool_weight,
    mlp_in,
    mlp_out,
):
    row_count, feature = points.shape
    offset = lax.axis_index("point") * row_count
    tree_rows = points.at[tree_order - offset].get(mode="promise_in_bounds", unique_indices=True)
    live_mask = (jnp.arange(BALL, dtype=jnp.int32)[None, :] < ball_counts[:, None]).reshape(-1)
    masked = ball_block(tree_rows, ball_counts, ball_proj, ball_out)
    chunk = MLP_CHUNK_ROWS
    refined = None
    for start in range(0, row_count, chunk):
        refined = mlp_block(masked, refined, start // MLP_BLOCK_ROWS, chunk // MLP_BLOCK_ROWS, mlp_in, mlp_out)
    pooled = jnp.einsum(
        "rjd,jde->re",
        masked.reshape(row_count // POOL, POOL, feature),
        pool_weight.reshape(POOL, feature, feature),
        preferred_element_type=jnp.float32,
    )
    device_count = lax.axis_size("point")
    level_count = device_count.bit_length() - 1
    coarse_state = pooled[None]
    for level_index in range(level_count):
        queries, key_rows, value_rows = coarse_qkv(coarse_state, coarse_proj)
        received = partner(jnp.stack([key_rows, value_rows]), "point", level_index)
        coarse_state = coarse_update(
            coarse_state,
            queries,
            jnp.concatenate([key_rows, received[0]], axis=1),
            jnp.concatenate([value_rows, received[1]], axis=1),
            coarse_out,
        )
    everyone = gather_all(coarse_state[0].astype(jnp.bfloat16), "point", GATHER_ORDER)
    summary = global_block(coarse_state[0], everyone, global_proj, global_out)
    unpooled = jnp.einsum(
        "rd,dje->jre",
        summary.reshape(-1, feature),
        unpool_weight.reshape(feature, POOL, feature),
        preferred_element_type=jnp.float32,
    )
    return final_block(ball_counts, refined, unpooled)


def solution(mesh):
    placed = (
        P(("dp", "point"), None),
        P(("dp", "point")),
        P(("dp", "point")),
        P(),
        P(),
        P(),
        P(),
        P(),
        P(),
        P(),
        P(),
        P(),
        P(),
    )
    return jax.shard_map(local_body, mesh=mesh, in_specs=placed, out_specs=P(("dp", "point"), None), check_vma=False)
```
